256 devices in a mesh: batch: 16 (over x_hi, z), dom: 16 (over x_lo, y, core).
Axes of the slice: x: 4 (x_hi: 2, x_lo: 2; x = x_hi * 2 + x_lo), y: 4, z: 8, core: 2. Of those that a mesh axis runs over, the one named last changes fastest.
Arguments:
- inputs: bfloat16 [32, 64, 68, 256], P('batch', 'dom'), may hold values from -70 to 70
- saved_q: bfloat16 [32, 64, 68, 256], P('batch', 'dom'), may hold values from -6.5 to 6.5
- saved_k: bfloat16 [32, 64, 68, 256], P('batch', 'dom'), may hold values from -6.5 to 6.5
- saved_v: bfloat16 [32, 64, 68, 256], P('batch', 'dom'), may hold values from -6 to 6
- attended: bfloat16 [32, 64, 68, 256], P('batch', 'dom'), may hold values from -6 to 6
- out_cot: bfloat16 [32, 64, 68, 256], P('batch', 'dom'), may hold values from -6 to 6
- conv_weight: bfloat16 [9, 256, 256], replicated, may hold values from -0.125 to 0.125
- qkv_weight: bfloat16 [256, 768], replicated, may hold values from -0.375 to 0.375
- out_weight: bfloat16 [256, 256], replicated, may hold values from -0.375 to 0.375
- norm_gain: float32 [256], replicated, may hold values from 0.5 to 1.5
- norm_shift: float32 [256], replicated, may hold values from -2.5 to 2.5
Outputs:
- input_grad: bfloat16 [32, 64, 68, 256], P('batch', 'dom')
- conv_grad: float32 [9, 256, 256], replicated
- qkv_grad: float32 [256, 768], replicated
- out_grad: float32 [256, 256], replicated
- gain_grad: float32 [256], replicated
- shift_grad: float32 [256], replicated
The draws below stay inside these ranges and needn't reach their ends.
All inputs are finite; a program needn't handle non-finite values.
Results may differ from the reference program's by a relative error of at most 0.011.
Values may be sent and summed in bfloat16 or wider, within the bound.
No kernel may reach another device: no remote copies, remote signals or barrier semaphores. Data moves between devices by JAX's collectives and lax.ppermute only.
A program may use at most 128 MiB of HBM per device.

```python
import jax
import jax.numpy as jnp
from jax import lax

C = 256
HEADS = 1
GROUPS = 32
W = 68
H = 64
B = 32


def attention_pair(key):
    shape = (B, H, W, C)
    first = jnp.clip(jax.random.normal(jax.random.fold_in(key, 1), shape, jnp.float32), -4.0, 4.0)
    second = jnp.clip(jax.random.normal(jax.random.fold_in(key, 2), shape, jnp.float32), -4.0, 4.0)
    return (first, second)


def draw_saved_q(key, part):
    return attention_pair(key)[0].astype(jnp.bfloat16)


def draw_saved_k(key, part):
    return attention_pair(key)[1].astype(jnp.bfloat16)


def draw_inputs(key, part):
    shape = (B, H, W, C)
    base = jnp.clip(jax.random.normal(jax.random.fold_in(key, 1), shape, jnp.float32), -4.0, 4.0)
    row_scale = 10.0 ** (jax.random.uniform(jax.random.fold_in(key, 2), (H,), jnp.float32) - 0.5)
    chan_scale = 10.0 ** (jax.random.uniform(jax.random.fold_in(key, 3), (C,), jnp.float32) - 0.5)
    position = jnp.arange(H).astype(jnp.float32) / max(H - 1, 1)
    ramp = 3.0 ** (position - 0.5)
    return (base * (row_scale * ramp)[None, :, None, None] * chan_scale).astype(jnp.bfloat16)


def steps_of(own_key, shape, shards, low, largest):
    loudness, own = 1.0, jax.random.fold_in(own_key, 6)
    for dim, blocks in shards:
        draws = jnp.exp(jax.random.uniform(jax.random.fold_in(own, dim), (blocks,), jnp.float32, low / len(shards), largest / len(shards)))
        loudness = loudness * jnp.repeat(draws, shape[dim] // blocks).reshape([-1 if axis == dim else 1 for axis in range(len(shape))])
    return loudness


def normal_values(own_key, dims, deviation, most, pieces=(), held_as=jnp.bfloat16):
    array = deviation * jax.random.normal(own_key, dims, jnp.float32)
    if pieces:
        array = array * steps_of(own_key, dims, pieces, -0.22, 0.18)
    return jnp.clip(array, -most, most).astype(held_as)


def setup_inputs(seed: int = 0) -> dict:
    arg_keys = jax.random.split(jax.random.key(seed), 12)
    return {
        "inputs": draw_inputs(jax.random.fold_in(arg_keys[11], 71), 0),
        "saved_q": draw_saved_q(jax.random.fold_in(arg_keys[11], 71), 0),
        "saved_k": draw_saved_k(jax.random.fold_in(arg_keys[11], 71), 0),
        "saved_v": normal_values(arg_keys[3], (B, H, W, C), 1.0, 6.0, ((0, 16), (1, 16))),
        "attended": normal_values(arg_keys[4], (B, H, W, C), 1.0, 6.0, ((0, 16), (1, 16))),
        "out_cot": normal_values(arg_keys[5], (B, H, W, C), 1.0, 6.0, ((0, 16), (1, 16))),
        "conv_weight": normal_values(arg_keys[6], (9, C, C), (9 * C) ** -0.5, 0.125),
        "qkv_weight": normal_values(arg_keys[7], (C, 3 * C), C ** -0.5, 0.375),
        "out_weight": normal_values(arg_keys[8], (C, C), C ** -0.5, 0.375),
        "norm_gain": jnp.clip(1.0 + 0.1 * jax.random.normal(arg_keys[9], (C,), jnp.float32), 0.5, 1.5),
        "norm_shift": normal_values(arg_keys[10], (C,), 0.5, 2.5, (), jnp.float32),
    }


EPSILON = 1e-05

def round_half(values):
    return lax.optimization_barrier(values.astype(jnp.bfloat16)).astype(jnp.float32)

def per_channel(values, group_width):
    return jnp.repeat(values, group_width, axis=-1)[:, None, None, :]

def attention_grads(operands):
    query, key_rows, value_rows, output_rows, d_output = operands
    seq_count = query.shape[0]
    head_width = C // HEADS
    score_scale = head_width ** (-0.5)

    def split_heads(values):
        return values.astype(jnp.float32).reshape(seq_count, HEADS, head_width)
    q_heads = split_heads(query)
    k_heads = split_heads(key_rows)
    v_heads = split_heads(value_rows)
    o_heads = split_heads(output_rows)
    do_heads = split_heads(d_output)
    logits = jnp.einsum('qhd,khd->hqk', q_heads, k_heads) * score_scale
    row_max = logits.max(-1, keepdims=True)
    log_norm = row_max + jnp.log(jnp.exp(logits - row_max).sum(-1, keepdims=True))
    softmax_p = jnp.exp(logits - log_norm)
    row_dot = jnp.einsum('qhd,qhd->hq', o_heads, do_heads)[..., None]
    d_probs = jnp.einsum('qhd,khd->hqk', do_heads, v_heads)
    d_scores = round_half(softmax_p * (d_probs - row_dot))
    d_query = (jnp.einsum('hqk,khd->qhd', d_scores, k_heads) * score_scale).astype(jnp.bfloat16)
    d_key = (jnp.einsum('hqk,qhd->khd', d_scores, q_heads) * score_scale).astype(jnp.bfloat16)
    d_value = jnp.einsum('hqk,qhd->khd', round_half(softmax_p), do_heads).astype(jnp.bfloat16)
    return jnp.concatenate([d_query.reshape(seq_count, C), d_key.reshape(seq_count, C), d_value.reshape(seq_count, C)], axis=-1)

def reference(inputs, saved_q, saved_k, saved_v, attended, out_cot, conv_weight, qkv_weight, out_weight, norm_gain, norm_shift):
    group_width = C // GROUPS
    count = H * W * group_width
    input_wide = inputs.astype(jnp.float32)
    grouped = input_wide.reshape(B, H, W, GROUPS, group_width)
    group_mean = grouped.sum((1, 2, 4)) / count
    group_var = (grouped * grouped).sum((1, 2, 4)) / count - group_mean * group_mean
    inv_std = lax.rsqrt(group_var + EPSILON)
    normed = (input_wide - per_channel(group_mean, group_width)) * per_channel(inv_std, group_width)
    pre_act = normed * norm_gain + norm_shift
    sigmoid_pre = jax.nn.sigmoid(pre_act)
    activated = (pre_act * sigmoid_pre).astype(jnp.bfloat16)
    padded = jnp.pad(activated, ((0, 0), (1, 1), (1, 1), (0, 0)))

    def shifted(source, row_start, col_start):
        return source[:, row_start:row_start + H, col_start:col_start + W, :].reshape(-1, C)
    conv_sum = input_wide.reshape(-1, C)
    for tap_index in range(9):
        row_off = tap_index // 3 - 1
        col_off = tap_index % 3 - 1
        conv_sum = conv_sum + jnp.dot(shifted(padded, 1 + row_off, 1 + col_off), conv_weight[tap_index], preferred_element_type=jnp.float32)
    residual = conv_sum.astype(jnp.bfloat16)
    out_flat = out_cot.reshape(-1, C)
    attended_flat = attended.reshape(-1, C)
    out_grad = jnp.dot(attended_flat.T, out_flat, preferred_element_type=jnp.float32)
    d_attended = jnp.dot(out_flat, out_weight.T, preferred_element_type=jnp.float32).astype(jnp.bfloat16)
    seq_count = H * W
    proj_grad = lax.map(attention_grads, (saved_q.reshape(B, seq_count, C), saved_k.reshape(B, seq_count, C), saved_v.reshape(B, seq_count, C), attended.reshape(B, seq_count, C), d_attended.reshape(B, seq_count, C)))
    proj_flat = proj_grad.reshape(-1, 3 * C)
    qkv_grad = jnp.dot(residual.T, proj_flat, preferred_element_type=jnp.float32)
    d_residual = (out_flat.astype(jnp.float32) + jnp.dot(proj_flat, qkv_weight.T, preferred_element_type=jnp.float32)).astype(jnp.bfloat16)
    d_padded = jnp.pad(d_residual.reshape(B, H, W, C), ((0, 0), (1, 1), (1, 1), (0, 0)))
    conv_parts = []
    d_act = jnp.zeros((B * H * W, C), jnp.float32)
    for tap_index in range(9):
        row_off = tap_index // 3 - 1
        col_off = tap_index % 3 - 1
        conv_parts.append(jnp.dot(shifted(padded, 1 + row_off, 1 + col_off).T, d_residual, preferred_element_type=jnp.float32))
        d_act = d_act + jnp.dot(shifted(d_padded, 1 - row_off, 1 - col_off), conv_weight[tap_index].T, preferred_element_type=jnp.float32)
    conv_grad = jnp.stack(conv_parts)
    d_pre = d_act.reshape(B, H, W, C) * sigmoid_pre * (1.0 + pre_act * (1.0 - sigmoid_pre))
    gain_grad = (d_pre * normed).sum((0, 1, 2))
    shift_grad = d_pre.sum((0, 1, 2))
    scaled = d_pre * norm_gain
    first = scaled.reshape(B, H, W, GROUPS, group_width).sum((1, 2, 4)) / count
    second = (scaled * normed).reshape(B, H, W, GROUPS, group_width).sum((1, 2, 4)) / count
    input_grad = (d_residual.reshape(B, H, W, C).astype(jnp.float32) + per_channel(inv_std, group_width) * (scaled - per_channel(first, group_width) - normed * per_channel(second, group_width))).astype(jnp.bfloat16)
    return (input_grad, conv_grad, qkv_grad, out_grad, gain_grad, shift_grad)
```

```python
import jax
import jax.numpy as jnp
from jax import lax
from jax.sharding import PartitionSpec as P

HEADS = 1
GROUPS = 32


EPSILON = 1e-05


def with_halo(cells, sides, width):
    for axis, dim in sides:
        count = lax.axis_size(axis)
        ends = count - 1
        head = lax.slice_in_dim(cells, 0, width, axis=dim)
        tail = lax.slice_in_dim(cells, cells.shape[dim] - width, cells.shape[dim], axis=dim)
        cells = jnp.concatenate(
            [
                lax.ppermute(tail, axis, [(i, (i + 1) % count) for i in range(ends)]),
                cells,
                lax.ppermute(head, axis, [((i + 1) % count, i) for i in range(ends)]),
            ],
            axis=dim,
        )
    return cells


def dom_psum(values):
    count = lax.axis_size("dom")
    step = 1
    while step < count:
        values = values + lax.ppermute(values, "dom", [(i, i ^ step) for i in range(count)])
        step *= 2
    return values


def dom_gather(values):
    count = lax.axis_size("dom")
    me = lax.axis_index("dom")
    values = values[None]
    step = 1
    while step < count:
        got = lax.ppermute(values, "dom", [(i, i ^ step) for i in range(count)])
        upper = (me // step) % 2 == 1
        values = jnp.where(
            upper, jnp.concatenate([got, values]), jnp.concatenate([values, got])
        )
        step *= 2
    return values


MESH_AXES = ("batch", "dom")
CORE0_BITS = (1, 3, 4, 2, 7, 5, 6)
CORE1_BITS = (4, 1, 3, 5, 2, 7, 6)


def mesh_psum(values):
    sizes = (lax.axis_size("batch"), lax.axis_size("dom"))
    if sizes != (16, 16):
        return lax.psum(values, MESH_AXES)
    count = 256
    me = lax.axis_index(MESH_AXES)
    core = me % 2
    steps = [(0, 0)] + list(zip(CORE0_BITS, CORE1_BITS))
    chosen = []
    for bit0, bit1 in steps:
        half = values.shape[0] // 2
        upper = jnp.where(core == 0, (me >> bit0) & 1, (me >> bit1) & 1) == 1
        low, high = values[:half], values[half:]
        send = jnp.where(upper, low, high)
        keep = jnp.where(upper, high, low)
        pairs = [(i, i ^ (1 << (bit0 if i % 2 == 0 else bit1))) for i in range(count)]
        values = keep + lax.ppermute(send, MESH_AXES, pairs)
        chosen.append((upper, pairs))
    for upper, pairs in reversed(chosen):
        got = lax.ppermute(values, MESH_AXES, pairs)
        values = jnp.where(
            upper, jnp.concatenate([got, values]), jnp.concatenate([values, got])
        )
    return values


def per_channel(values, group_width):
    return jnp.repeat(values, group_width, axis=-1)[:, None, None, :]


def body(
    inputs,
    saved_q,
    saved_k,
    saved_v,
    attended,
    out_cot,
    conv_weight,
    qkv_weight,
    out_weight,
    norm_gain,
    norm_shift,
):
    samples, row_count, col_count, chan_count = inputs.shape
    tok_count = row_count * col_count
    group_width = chan_count // GROUPS
    head_width = chan_count // HEADS
    score_scale = head_width ** (-0.5)
    count = row_count * col_count * group_width * lax.axis_size("dom")
    f32 = jnp.float32
    bf16 = jnp.bfloat16
    input_wide = inputs.astype(f32)
    grouped = input_wide.reshape(samples, row_count, col_count, GROUPS, group_width)
    group_sums = dom_psum(jnp.stack([grouped.sum((1, 2, 4)), (grouped * grouped).sum((1, 2, 4))]))
    group_mean = group_sums[0] / count
    group_var = group_sums[1] / count - group_mean * group_mean
    inv_std = lax.rsqrt(group_var + EPSILON)
    normed = (input_wide - per_channel(group_mean, group_width)) * per_channel(inv_std, group_width)
    pre_act = normed * norm_gain + norm_shift
    sigmoid_pre = jax.nn.sigmoid(pre_act)
    activated = (pre_act * sigmoid_pre).astype(bf16)
    padded = with_halo(activated, (("dom", 1),), 1)
    padded = jnp.pad(padded, ((0, 0), (0, 0), (1, 1), (0, 0)))

    def shifted(source, row_start, col_start):
        return source[
            :, row_start : row_start + row_count, col_start : col_start + col_count, :
        ].reshape(-1, chan_count)

    conv_sum = input_wide.reshape(-1, chan_count)
    for tap_index in range(9):
        row_off = tap_index // 3 - 1
        col_off = tap_index % 3 - 1
        conv_sum = conv_sum + jnp.dot(
            shifted(padded, 1 + row_off, 1 + col_off),
            conv_weight[tap_index],
            preferred_element_type=f32,
        )
    residual = conv_sum.astype(bf16)
    out_flat = out_cot.reshape(-1, chan_count)
    attended_flat = attended.reshape(-1, chan_count)
    out_grad = jnp.einsum("nc,nd->cd", attended_flat, out_flat, preferred_element_type=f32)
    d_attended = jnp.einsum("nd,cd->nc", out_flat, out_weight, preferred_element_type=f32).astype(
        bf16
    )

    def split_heads(values):
        return values.reshape(samples, -1, HEADS, head_width)

    def scores(left, right):
        return jnp.einsum("sqhd,skhd->shqk", left, right, preferred_element_type=f32) * score_scale

    q_rows = saved_q.reshape(samples, tok_count, chan_count)
    k_rows = saved_k.reshape(samples, tok_count, chan_count)
    v_rows = saved_v.reshape(samples, tok_count, chan_count)
    do_rows = d_attended.reshape(samples, tok_count, chan_count)
    q_heads = split_heads(q_rows)
    k_heads = split_heads(k_rows)
    v_heads = split_heads(v_rows)
    do_heads = split_heads(do_rows)
    row_dot = jnp.einsum(
        "sqhd,sqhd->sqh",
        split_heads(attended.reshape(samples, tok_count, chan_count)),
        do_heads,
        preferred_element_type=f32,
    )
    row_dot_t = row_dot.transpose(0, 2, 1)

    def grad_terms(query_heads, dout_heads, key_heads, value_heads, log_norm_t, dot_t):
        softmax_p = jnp.exp(scores(query_heads, key_heads) - log_norm_t[..., None])
        d_probs = jnp.einsum("sqhd,skhd->shqk", dout_heads, value_heads, preferred_element_type=f32)
        d_scores = (softmax_p * (d_probs - dot_t[..., None])).astype(bf16)
        return (softmax_p.astype(bf16), d_scores)

    row_max = jnp.full((samples, HEADS, tok_count), -jnp.inf, f32)
    row_total = jnp.zeros((samples, HEADS, tok_count), f32)
    logits = scores(q_heads, split_heads(lax.all_gather(k_rows, "dom", axis=1, tiled=True)))
    new_max = logits.max(-1)
    row_total = row_total * jnp.exp(row_max - new_max) + jnp.exp(logits - new_max[..., None]).sum(
        -1
    )
    row_max, row_total = (new_max, row_total)
    log_norm = row_max + jnp.log(row_total)
    shard_piece = (
        lax.all_gather(k_rows, "dom", axis=1, tiled=True),
        lax.all_gather(v_rows, "dom", axis=1, tiled=True),
    )
    key_heads = split_heads(shard_piece[0])
    value_heads = split_heads(shard_piece[1])
    p_half, d_scores = grad_terms(q_heads, do_heads, key_heads, value_heads, log_norm, row_dot_t)
    q_accum = jnp.einsum("shqk,skhd->sqhd", d_scores, key_heads, preferred_element_type=f32)
    stats_local = dom_gather(jnp.stack([log_norm.transpose(0, 2, 1), row_dot]))
    stats_all = stats_local.transpose(1, 2, 0, 3, 4).reshape(2, samples, -1, HEADS)
    shard_piece = (
        lax.all_gather(q_rows, "dom", axis=1, tiled=True),
        lax.all_gather(do_rows, "dom", axis=1, tiled=True),
    )
    query_heads = split_heads(shard_piece[0])
    dout_heads = split_heads(shard_piece[1])
    norm_piece = stats_all[0].transpose(0, 2, 1)
    dot_piece = stats_all[1].transpose(0, 2, 1)
    p_half, d_scores = grad_terms(query_heads, dout_heads, k_heads, v_heads, norm_piece, dot_piece)
    k_accum = jnp.einsum("shqk,sqhd->skhd", d_scores, query_heads, preferred_element_type=f32)
    v_accum = jnp.einsum("shqk,sqhd->skhd", p_half, dout_heads, preferred_element_type=f32)
    k_accum, v_accum = (k_accum, v_accum)
    k_grad = (k_accum * score_scale).astype(bf16).reshape(samples, tok_count, chan_count)
    v_grad = v_accum.astype(bf16).reshape(samples, tok_count, chan_count)
    q_grad = (q_accum * score_scale).astype(bf16).reshape(samples, tok_count, chan_count)
    proj_grad = jnp.concatenate([q_grad, k_grad, v_grad], axis=-1).reshape(-1, 3 * chan_count)
    qkv_local = jnp.einsum("nc,nd->cd", residual, proj_grad, preferred_element_type=f32)
    d_residual = (
        out_flat.astype(f32)
        + jnp.einsum("nd,cd->nc", proj_grad, qkv_weight, preferred_element_type=f32)
    ).astype(bf16)
    d_res_map = d_residual.reshape(samples, row_count, col_count, chan_count)
    d_padded = with_halo(d_res_map, (("dom", 1),), 1)
    d_padded = jnp.pad(d_padded, ((0, 0), (0, 0), (1, 1), (0, 0)))
    conv_parts = []
    d_act = jnp.zeros((samples * tok_count, chan_count), f32)
    for tap_index in range(9):
        row_off = tap_index // 3 - 1
        col_off = tap_index % 3 - 1
        conv_parts.append(
            jnp.einsum(
                "nc,nd->cd",
                shifted(padded, 1 + row_off, 1 + col_off),
                d_residual,
                preferred_element_type=f32,
            )
        )
        d_act = d_act + jnp.einsum(
            "nd,cd->nc",
            shifted(d_padded, 1 - row_off, 1 - col_off),
            conv_weight[tap_index],
            preferred_element_type=f32,
        )
    conv_local = jnp.stack(conv_parts)
    d_pre = (
        d_act.reshape(samples, row_count, col_count, chan_count)
        * sigmoid_pre
        * (1.0 + pre_act * (1.0 - sigmoid_pre))
    )
    gain_local = (d_pre * normed).sum((0, 1, 2))
    shift_local = d_pre.sum((0, 1, 2))
    scaled = d_pre * norm_gain
    scaled_groups = scaled.reshape(samples, row_count, col_count, GROUPS, group_width)
    product_groups = (scaled * normed).reshape(samples, row_count, col_count, GROUPS, group_width)
    back_sums = dom_psum(jnp.stack([scaled_groups.sum((1, 2, 4)), product_groups.sum((1, 2, 4))]))
    first = back_sums[0] / count
    second = back_sums[1] / count
    input_grad = (
        d_res_map.astype(f32)
        + per_channel(inv_std, group_width)
        * (scaled - per_channel(first, group_width) - normed * per_channel(second, group_width))
    ).astype(bf16)
    parts = (out_grad, qkv_local, conv_local, gain_local, shift_local)
    flat = jnp.concatenate([part.reshape(-1) for part in parts])
    total = flat.shape[0]
    padded_len = -(-total // 32768) * 32768
    flat = mesh_psum(jnp.pad(flat, (0, padded_len - total)))
    pieces = []
    offset = 0
    for part in parts:
        pieces.append(flat[offset : offset + part.size].reshape(part.shape))
        offset += part.size
    out_grad, qkv_grad, conv_grad, gain_grad, shift_grad = pieces
    return (input_grad, conv_grad, qkv_grad, out_grad, gain_grad, shift_grad)


def solution(mesh):
    placed = (
        P("batch", "dom", None, None),
        P("batch", "dom", None, None),
        P("batch", "dom", None, None),
        P("batch", "dom", None, None),
        P("batch", "dom", None, None),
        P("batch", "dom", None, None),
        P(),
        P(),
        P(),
        P(),
        P(),
    )
    return jax.shard_map(
        body,
        mesh=mesh,
        in_specs=placed,
        out_specs=(P("batch", "dom", None, None), P(), P(), P(), P(), P()),
        check_vma=False,
    )
```

```python
import jax
import jax.numpy as jnp
from jax import lax
from jax.sharding import PartitionSpec as P

HEADS = 1
GROUPS = 32


EPSILON = 1e-05


def with_halo(cells, sides, width):
    for axis, dim in sides:
        count = lax.axis_size(axis)
        ends = count - 1
        head = lax.slice_in_dim(cells, 0, width, axis=dim)
        tail = lax.slice_in_dim(cells, cells.shape[dim] - width, cells.shape[dim], axis=dim)
        cells = jnp.concatenate(
            [
                lax.ppermute(tail, axis, [(i, (i + 1) % count) for i in range(ends)]),
                cells,
                lax.ppermute(head, axis, [((i + 1) % count, i) for i in range(ends)]),
            ],
            axis=dim,
        )
    return cells


def dom_psum(values):
    count = lax.axis_size("dom")
    step = 1
    while step < count:
        values = values + lax.ppermute(values, "dom", [(i, i ^ step) for i in range(count)])
        step *= 2
    return values


def dom_gather(values):
    count = lax.axis_size("dom")
    me = lax.axis_index("dom")
    values = values[None]
    step = 1
    while step < count:
        got = lax.ppermute(values, "dom", [(i, i ^ step) for i in range(count)])
        upper = (me // step) % 2 == 1
        values = jnp.where(
            upper, jnp.concatenate([got, values]), jnp.concatenate([values, got])
        )
        step *= 2
    return values


MESH_AXES = ("batch", "dom")
CORE0_BITS = (1, 3, 4, 2, 7, 5, 6)
CORE1_BITS = (4, 1, 3, 5, 2, 7, 6)


def mesh_psum(values):
    sizes = (lax.axis_size("batch"), lax.axis_size("dom"))
    if sizes != (16, 16):
        return lax.psum(values, MESH_AXES)
    count = 256
    me = lax.axis_index(MESH_AXES)
    core = me % 2
    steps = [(0, 0)] + list(zip(CORE0_BITS, CORE1_BITS))
    chosen = []
    for bit0, bit1 in steps:
        half = values.shape[0] // 2
        upper = jnp.where(core == 0, (me >> bit0) & 1, (me >> bit1) & 1) == 1
        low, high = values[:half], values[half:]
        send = jnp.where(upper, low, high)
        keep = jnp.where(upper, high, low)
        pairs = [(i, i ^ (1 << (bit0 if i % 2 == 0 else bit1))) for i in range(count)]
        values = keep + lax.ppermute(send, MESH_AXES, pairs)
        chosen.append((upper, pairs))
    for upper, pairs in reversed(chosen):
        got = lax.ppermute(values, MESH_AXES, pairs)
        values = jnp.where(
            upper, jnp.concatenate([got, values]), jnp.concatenate([values, got])
        )
    return values


def per_channel(values, group_width):
    return jnp.repeat(values, group_width, axis=-1)[:, None, None, :]


def body(
    inputs,
    saved_q,
    saved_k,
    saved_v,
    attended,
    out_cot,
    conv_weight,
    qkv_weight,
    out_weight,
    norm_gain,
    norm_shift,
):
    samples, row_count, col_count, chan_count = inputs.shape
    tok_count = row_count * col_count
    group_width = chan_count // GROUPS
    head_width = chan_count // HEADS
    score_scale = head_width ** (-0.5)
    count = row_count * col_count * group_width * lax.axis_size("dom")
    f32 = jnp.float32
    bf16 = jnp.bfloat16
    input_wide = inputs.astype(f32)
    grouped = input_wide.reshape(samples, row_count, col_count, GROUPS, group_width)
    group_sums = dom_psum(jnp.stack([grouped.sum((1, 2, 4)), (grouped * grouped).sum((1, 2, 4))]))
    group_mean = group_sums[0] / count
    group_var = group_sums[1] / count - group_mean * group_mean
    inv_std = lax.rsqrt(group_var + EPSILON)
    normed = (input_wide - per_channel(group_mean, group_width)) * per_channel(inv_std, group_width)
    pre_act = normed * norm_gain + norm_shift
    sigmoid_pre = jax.nn.sigmoid(pre_act)
    activated = (pre_act * sigmoid_pre).astype(bf16)
    padded = with_halo(activated, (("dom", 1),), 1)
    padded = jnp.pad(padded, ((0, 0), (0, 0), (1, 1), (0, 0)))

    def shifted(source, row_start, col_start):
        return source[
            :, row_start : row_start + row_count, col_start : col_start + col_count, :
        ].reshape(-1, chan_count)

    conv_sum = input_wide.reshape(-1, chan_count)
    for tap_index in range(9):
        row_off = tap_index // 3 - 1
        col_off = tap_index % 3 - 1
        conv_sum = conv_sum + jnp.dot(
            shifted(padded, 1 + row_off, 1 + col_off),
            conv_weight[tap_index],
            preferred_element_type=f32,
        )
    residual = conv_sum.astype(bf16)
    out_flat = out_cot.reshape(-1, chan_count)
    attended_flat = attended.reshape(-1, chan_count)
    out_grad = jnp.einsum("nc,nd->cd", attended_flat, out_flat, preferred_element_type=f32)
    d_attended = jnp.einsum("nd,cd->nc", out_flat, out_weight, preferred_element_type=f32).astype(
        bf16
    )

    def split_heads(values):
        return values.reshape(samples, -1, HEADS, head_width)

    def scores(left, right):
        return jnp.einsum("sqhd,skhd->shqk", left, right, preferred_element_type=f32) * score_scale

    q_rows = saved_q.reshape(samples, tok_count, chan_count)
    k_rows = saved_k.reshape(samples, tok_count, chan_count)
    v_rows = saved_v.reshape(samples, tok_count, chan_count)
    do_rows = d_attended.reshape(samples, tok_count, chan_count)
    q_heads = split_heads(q_rows)
    k_heads = split_heads(k_rows)
    v_heads = split_heads(v_rows)
    do_heads = split_heads(do_rows)
    row_dot = jnp.einsum(
        "sqhd,sqhd->sqh",
        split_heads(attended.reshape(samples, tok_count, chan_count)),
        do_heads,
        preferred_element_type=f32,
    )
    row_dot_t = row_dot.transpose(0, 2, 1)

    def grad_terms(query_heads, dout_heads, key_heads, value_heads, log_norm_t, dot_t):
        softmax_p = jnp.exp(scores(query_heads, key_heads) - log_norm_t[..., None])
        d_probs = jnp.einsum("sqhd,skhd->shqk", dout_heads, value_heads, preferred_element_type=f32)
        d_scores = (softmax_p * (d_probs - dot_t[..., None])).astype(bf16)
        return (softmax_p.astype(bf16), d_scores)

    row_max = jnp.full((samples, HEADS, tok_count), -jnp.inf, f32)
    row_total = jnp.zeros((samples, HEADS, tok_count), f32)
    k_all = lax.all_gather(k_rows, "dom", axis=1, tiled=True)
    residual, padded, k_all = lax.optimization_barrier((residual, padded, k_all))
    logits = scores(q_heads, split_heads(k_all))
    new_max = logits.max(-1)
    row_total = row_total * jnp.exp(row_max - new_max) + jnp.exp(logits - new_max[..., None]).sum(
        -1
    )
    row_max, row_total = (new_max, row_total)
    log_norm = row_max + jnp.log(row_total)
    shard_piece = (
        k_all,
        lax.all_gather(v_rows, "dom", axis=1, tiled=True),
    )
    key_heads = split_heads(shard_piece[0])
    value_heads = split_heads(shard_piece[1])
    p_half, d_scores = grad_terms(q_heads, do_heads, key_heads, value_heads, log_norm, row_dot_t)
    q_accum = jnp.einsum("shqk,skhd->sqhd", d_scores, key_heads, preferred_element_type=f32)
    stats_local = dom_gather(jnp.stack([log_norm.transpose(0, 2, 1), row_dot]))
    stats_all = stats_local.transpose(1, 2, 0, 3, 4).reshape(2, samples, -1, HEADS)
    shard_piece = (
        lax.all_gather(q_rows, "dom", axis=1, tiled=True),
        lax.all_gather(do_rows, "dom", axis=1, tiled=True),
    )
    query_heads = split_heads(shard_piece[0])
    dout_heads = split_heads(shard_piece[1])
    norm_piece = stats_all[0].transpose(0, 2, 1)
    dot_piece = stats_all[1].transpose(0, 2, 1)
    p_half, d_scores = grad_terms(query_heads, dout_heads, k_heads, v_heads, norm_piece, dot_piece)
    k_accum = jnp.einsum("shqk,sqhd->skhd", d_scores, query_heads, preferred_element_type=f32)
    v_accum = jnp.einsum("shqk,sqhd->skhd", p_half, dout_heads, preferred_element_type=f32)
    k_accum, v_accum = (k_accum, v_accum)
    k_grad = (k_accum * score_scale).astype(bf16).reshape(samples, tok_count, chan_count)
    v_grad = v_accum.astype(bf16).reshape(samples, tok_count, chan_count)
    q_grad = (q_accum * score_scale).astype(bf16).reshape(samples, tok_count, chan_count)
    proj_grad = jnp.concatenate([q_grad, k_grad, v_grad], axis=-1).reshape(-1, 3 * chan_count)
    qkv_local = jnp.einsum("nc,nd->cd", residual, proj_grad, preferred_element_type=f32)
    d_residual = (
        out_flat.astype(f32)
        + jnp.einsum("nd,cd->nc", proj_grad, qkv_weight, preferred_element_type=f32)
    ).astype(bf16)
    d_res_map = d_residual.reshape(samples, row_count, col_count, chan_count)
    d_padded = with_halo(d_res_map, (("dom", 1),), 1)
    d_padded = jnp.pad(d_padded, ((0, 0), (0, 0), (1, 1), (0, 0)))
    conv_parts = []
    d_act = jnp.zeros((samples * tok_count, chan_count), f32)
    for tap_index in range(9):
        row_off = tap_index // 3 - 1
        col_off = tap_index % 3 - 1
        conv_parts.append(
            jnp.einsum(
                "nc,nd->cd",
                shifted(padded, 1 + row_off, 1 + col_off),
                d_residual,
                preferred_element_type=f32,
            )
        )
        d_act = d_act + jnp.einsum(
            "nd,cd->nc",
            shifted(d_padded, 1 - row_off, 1 - col_off),
            conv_weight[tap_index],
            preferred_element_type=f32,
        )
    conv_local = jnp.stack(conv_parts)
    d_pre = (
        d_act.reshape(samples, row_count, col_count, chan_count)
        * sigmoid_pre
        * (1.0 + pre_act * (1.0 - sigmoid_pre))
    )
    gain_local = (d_pre * normed).sum((0, 1, 2))
    shift_local = d_pre.sum((0, 1, 2))
    scaled = d_pre * norm_gain
    scaled_groups = scaled.reshape(samples, row_count, col_count, GROUPS, group_width)
    product_groups = (scaled * normed).reshape(samples, row_count, col_count, GROUPS, group_width)
    back_sums = dom_psum(jnp.stack([scaled_groups.sum((1, 2, 4)), product_groups.sum((1, 2, 4))]))
    parts = (out_grad, qkv_local, conv_local, gain_local, shift_local)
    flat = jnp.concatenate([part.reshape(-1) for part in parts])
    flat, back_sums = lax.optimization_barrier((flat, back_sums))
    first = back_sums[0] / count
    second = back_sums[1] / count
    input_grad = (
        d_res_map.astype(f32)
        + per_channel(inv_std, group_width)
        * (scaled - per_channel(first, group_width) - normed * per_channel(second, group_width))
    ).astype(bf16)
    total = flat.shape[0]
    padded_len = -(-total // 32768) * 32768
    flat = mesh_psum(jnp.pad(flat, (0, padded_len - total)))
    pieces = []
    offset = 0
    for part in parts:
        pieces.append(flat[offset : offset + part.size].reshape(part.shape))
        offset += part.size
    out_grad, qkv_grad, conv_grad, gain_grad, shift_grad = pieces
    return (input_grad, conv_grad, qkv_grad, out_grad, gain_grad, shift_grad)


def solution(mesh):
    placed = (
        P("batch", "dom", None, None),
        P("batch", "dom", None, None),
        P("batch", "dom", None, None),
        P("batch", "dom", None, None),
        P("batch", "dom", None, None),
        P("batch", "dom", None, None),
        P(),
        P(),
        P(),
        P(),
        P(),
    )
    return jax.shard_map(
        body,
        mesh=mesh,
        in_specs=placed,
        out_specs=(P("batch", "dom", None, None), P(), P(), P(), P(), P()),
        check_vma=False,
    )
```

```python
import jax
import jax.numpy as jnp
from jax import lax
from jax.sharding import PartitionSpec as P

HEADS = 1
GROUPS = 32


EPSILON = 1e-05


def with_halo(cells, sides, width):
    for axis, dim in sides:
        count = lax.axis_size(axis)
        ends = count - 1
        head = lax.slice_in_dim(cells, 0, width, axis=dim)
        tail = lax.slice_in_dim(cells, cells.shape[dim] - width, cells.shape[dim], axis=dim)
        cells = jnp.concatenate(
            [
                lax.ppermute(tail, axis, [(i, (i + 1) % count) for i in range(ends)]),
                cells,
                lax.ppermute(head, axis, [((i + 1) % count, i) for i in range(ends)]),
            ],
            axis=dim,
        )
    return cells


def dom_psum(values):
    count = lax.axis_size("dom")
    step = 1
    while step < count:
        values = values + lax.ppermute(values, "dom", [(i, i ^ step) for i in range(count)])
        step *= 2
    return values


def dom_gather(values):
    count = lax.axis_size("dom")
    me = lax.axis_index("dom")
    values = values[None]
    step = 1
    while step < count:
        got = lax.ppermute(values, "dom", [(i, i ^ step) for i in range(count)])
        upper = (me // step) % 2 == 1
        values = jnp.where(
            upper, jnp.concatenate([got, values]), jnp.concatenate([values, got])
        )
        step *= 2
    return values


MESH_AXES = ("batch", "dom")
CORE0_BITS = (1, 3, 4, 2, 7, 5, 6)
CORE1_BITS = (4, 1, 3, 5, 2, 7, 6)


def mesh_psum(values):
    sizes = (lax.axis_size("batch"), lax.axis_size("dom"))
    if sizes != (16, 16):
        return lax.psum(values, MESH_AXES)
    count = 256
    me = lax.axis_index(MESH_AXES)
    core = me % 2
    steps = [(0, 0)] + list(zip(CORE0_BITS, CORE1_BITS))
    chosen = []
    for bit0, bit1 in steps:
        half = values.shape[0] // 2
        upper = jnp.where(core == 0, (me >> bit0) & 1, (me >> bit1) & 1) == 1
        low, high = values[:half], values[half:]
        send = jnp.where(upper, low, high)
        keep = jnp.where(upper, high, low)
        pairs = [(i, i ^ (1 << (bit0 if i % 2 == 0 else bit1))) for i in range(count)]
        values = keep + lax.ppermute(send, MESH_AXES, pairs)
        chosen.append((upper, pairs))
    for upper, pairs in reversed(chosen):
        got = lax.ppermute(values, MESH_AXES, pairs)
        values = jnp.where(
            upper, jnp.concatenate([got, values]), jnp.concatenate([values, got])
        )
    return values


def per_channel(values, group_width):
    return jnp.repeat(values, group_width, axis=-1)[:, None, None, :]


def body(
    inputs,
    saved_q,
    saved_k,
    saved_v,
    attended,
    out_cot,
    conv_weight,
    qkv_weight,
    out_weight,
    norm_gain,
    norm_shift,
):
    samples, row_count, col_count, chan_count = inputs.shape
    tok_count = row_count * col_count
    group_width = chan_count // GROUPS
    head_width = chan_count // HEADS
    score_scale = head_width ** (-0.5)
    count = row_count * col_count * group_width * lax.axis_size("dom")
    f32 = jnp.float32
    bf16 = jnp.bfloat16
    input_wide = inputs.astype(f32)
    grouped = input_wide.reshape(samples, row_count, col_count, GROUPS, group_width)
    group_sums = dom_psum(jnp.stack([grouped.sum((1, 2, 4)), (grouped * grouped).sum((1, 2, 4))]))
    group_mean = group_sums[0] / count
    group_var = group_sums[1] / count - group_mean * group_mean
    inv_std = lax.rsqrt(group_var + EPSILON)
    normed = (input_wide - per_channel(group_mean, group_width)) * per_channel(inv_std, group_width)
    pre_act = normed * norm_gain + norm_shift
    sigmoid_pre = jax.nn.sigmoid(pre_act)
    activated = (pre_act * sigmoid_pre).astype(bf16)
    padded = with_halo(activated, (("dom", 1),), 1)
    padded = jnp.pad(padded, ((0, 0), (0, 0), (1, 1), (0, 0)))

    def shifted(source, row_start, col_start):
        return source[
            :, row_start : row_start + row_count, col_start : col_start + col_count, :
        ].reshape(-1, chan_count)

    conv_sum = input_wide.reshape(-1, chan_count)
    for tap_index in range(9):
        row_off = tap_index // 3 - 1
        col_off = tap_index % 3 - 1
        conv_sum = conv_sum + jnp.dot(
            shifted(padded, 1 + row_off, 1 + col_off),
            conv_weight[tap_index],
            preferred_element_type=f32,
        )
    residual = conv_sum.astype(bf16)
    out_flat = out_cot.reshape(-1, chan_count)
    attended_flat = attended.reshape(-1, chan_count)
    out_grad = jnp.einsum("nc,nd->cd", attended_flat, out_flat, preferred_element_type=f32)
    d_attended = jnp.einsum("nd,cd->nc", out_flat, out_weight, preferred_element_type=f32).astype(
        bf16
    )

    def split_heads(values):
        return values.reshape(samples, -1, HEADS, head_width)

    def scores(left, right):
        return jnp.einsum("sqhd,skhd->shqk", left, right, preferred_element_type=f32) * score_scale

    q_rows = saved_q.reshape(samples, tok_count, chan_count)
    k_rows = saved_k.reshape(samples, tok_count, chan_count)
    v_rows = saved_v.reshape(samples, tok_count, chan_count)
    do_rows = d_attended.reshape(samples, tok_count, chan_count)
    q_heads = split_heads(q_rows)
    k_heads = split_heads(k_rows)
    v_heads = split_heads(v_rows)
    do_heads = split_heads(do_rows)
    row_dot = jnp.einsum(
        "sqhd,sqhd->sqh",
        split_heads(attended.reshape(samples, tok_count, chan_count)),
        do_heads,
        preferred_element_type=f32,
    )
    row_dot_t = row_dot.transpose(0, 2, 1)

    def grad_terms(query_heads, dout_heads, key_heads, value_heads, log_norm_t, dot_t):
        softmax_p = jnp.exp(scores(query_heads, key_heads) - log_norm_t[..., None])
        d_probs = jnp.einsum("sqhd,skhd->shqk", dout_heads, value_heads, preferred_element_type=f32)
        d_scores = (softmax_p * (d_probs - dot_t[..., None])).astype(bf16)
        return (softmax_p.astype(bf16), d_scores)

    row_max = jnp.full((samples, HEADS, tok_count), -jnp.inf, f32)
    row_total = jnp.zeros((samples, HEADS, tok_count), f32)
    kv_all = lax.all_gather(jnp.stack([k_rows, v_rows]), "dom", axis=2, tiled=True)
    residual, padded, kv_all = lax.optimization_barrier((residual, padded, kv_all))
    k_all = kv_all[0]
    logits = scores(q_heads, split_heads(k_all))
    new_max = logits.max(-1)
    row_total = row_total * jnp.exp(row_max - new_max) + jnp.exp(logits - new_max[..., None]).sum(
        -1
    )
    row_max, row_total = (new_max, row_total)
    log_norm = row_max + jnp.log(row_total)
    shard_piece = (
        k_all,
        kv_all[1],
    )
    key_heads = split_heads(shard_piece[0])
    value_heads = split_heads(shard_piece[1])
    p_half, d_scores = grad_terms(q_heads, do_heads, key_heads, value_heads, log_norm, row_dot_t)
    q_accum = jnp.einsum("shqk,skhd->sqhd", d_scores, key_heads, preferred_element_type=f32)
    stats_local = dom_gather(jnp.stack([log_norm.transpose(0, 2, 1), row_dot]))
    stats_all = stats_local.transpose(1, 2, 0, 3, 4).reshape(2, samples, -1, HEADS)
    qdo_all = lax.all_gather(jnp.stack([q_rows, do_rows]), "dom", axis=2, tiled=True)
    shard_piece = (qdo_all[0], qdo_all[1])
    query_heads = split_heads(shard_piece[0])
    dout_heads = split_heads(shard_piece[1])
    norm_piece = stats_all[0].transpose(0, 2, 1)
    dot_piece = stats_all[1].transpose(0, 2, 1)
    p_half, d_scores = grad_terms(query_heads, dout_heads, k_heads, v_heads, norm_piece, dot_piece)
    k_accum = jnp.einsum("shqk,sqhd->skhd", d_scores, query_heads, preferred_element_type=f32)
    v_accum = jnp.einsum("shqk,sqhd->skhd", p_half, dout_heads, preferred_element_type=f32)
    k_accum, v_accum = (k_accum, v_accum)
    k_grad = (k_accum * score_scale).astype(bf16).reshape(samples, tok_count, chan_count)
    v_grad = v_accum.astype(bf16).reshape(samples, tok_count, chan_count)
    q_grad = (q_accum * score_scale).astype(bf16).reshape(samples, tok_count, chan_count)
    proj_grad = jnp.concatenate([q_grad, k_grad, v_grad], axis=-1).reshape(-1, 3 * chan_count)
    qkv_local = jnp.einsum("nc,nd->cd", residual, proj_grad, preferred_element_type=f32)
    d_residual = (
        out_flat.astype(f32)
        + jnp.einsum("nd,cd->nc", proj_grad, qkv_weight, preferred_element_type=f32)
    ).astype(bf16)
    d_res_map = d_residual.reshape(samples, row_count, col_count, chan_count)
    d_padded = with_halo(d_res_map, (("dom", 1),), 1)
    d_padded = jnp.pad(d_padded, ((0, 0), (0, 0), (1, 1), (0, 0)))
    conv_parts = []
    d_act = jnp.zeros((samples * tok_count, chan_count), f32)
    for tap_index in range(9):
        row_off = tap_index // 3 - 1
        col_off = tap_index % 3 - 1
        conv_parts.append(
            jnp.einsum(
                "nc,nd->cd",
                shifted(padded, 1 + row_off, 1 + col_off),
                d_residual,
                preferred_element_type=f32,
            )
        )
        d_act = d_act + jnp.einsum(
            "nd,cd->nc",
            shifted(d_padded, 1 - row_off, 1 - col_off),
            conv_weight[tap_index],
            preferred_element_type=f32,
        )
    conv_local = jnp.stack(conv_parts)
    d_pre = (
        d_act.reshape(samples, row_count, col_count, chan_count)
        * sigmoid_pre
        * (1.0 + pre_act * (1.0 - sigmoid_pre))
    )
    gain_local = (d_pre * normed).sum((0, 1, 2))
    shift_local = d_pre.sum((0, 1, 2))
    scaled = d_pre * norm_gain
    scaled_groups = scaled.reshape(samples, row_count, col_count, GROUPS, group_width)
    product_groups = (scaled * normed).reshape(samples, row_count, col_count, GROUPS, group_width)
    back_sums = dom_psum(jnp.stack([scaled_groups.sum((1, 2, 4)), product_groups.sum((1, 2, 4))]))
    parts = (out_grad, qkv_local, conv_local, gain_local, shift_local)
    flat = jnp.concatenate([part.reshape(-1) for part in parts])
    flat, back_sums = lax.optimization_barrier((flat, back_sums))
    first = back_sums[0] / count
    second = back_sums[1] / count
    input_grad = (
        d_res_map.astype(f32)
        + per_channel(inv_std, group_width)
        * (scaled - per_channel(first, group_width) - normed * per_channel(second, group_width))
    ).astype(bf16)
    total = flat.shape[0]
    padded_len = -(-total // 32768) * 32768
    flat = mesh_psum(jnp.pad(flat, (0, padded_len - total)))
    pieces = []
    offset = 0
    for part in parts:
        pieces.append(flat[offset : offset + part.size].reshape(part.shape))
        offset += part.size
    out_grad, qkv_grad, conv_grad, gain_grad, shift_grad = pieces
    return (input_grad, conv_grad, qkv_grad, out_grad, gain_grad, shift_grad)


def solution(mesh):
    placed = (
        P("batch", "dom", None, None),
        P("batch", "dom", None, None),
        P("batch", "dom", None, None),
        P("batch", "dom", None, None),
        P("batch", "dom", None, None),
        P("batch", "dom", None, None),
        P(),
        P(),
        P(),
        P(),
        P(),
    )
    return jax.shard_map(
        body,
        mesh=mesh,
        in_specs=placed,
        out_specs=(P("batch", "dom", None, None), P(), P(), P(), P(), P()),
        check_vma=False,
    )
```

```python
import jax
import jax.numpy as jnp
from jax import lax
from jax.sharding import PartitionSpec as P

HEADS = 1
GROUPS = 32


EPSILON = 1e-05


def with_halo(cells, sides, width):
    for axis, dim in sides:
        count = lax.axis_size(axis)
        ends = count - 1
        head = lax.slice_in_dim(cells, 0, width, axis=dim)
        tail = lax.slice_in_dim(cells, cells.shape[dim] - width, cells.shape[dim], axis=dim)
        cells = jnp.concatenate(
            [
                lax.ppermute(tail, axis, [(i, (i + 1) % count) for i in range(ends)]),
                cells,
                lax.ppermute(head, axis, [((i + 1) % count, i) for i in range(ends)]),
            ],
            axis=dim,
        )
    return cells


def dom_psum(values):
    count = lax.axis_size("dom")
    step = 1
    while step < count:
        values = values + lax.ppermute(values, "dom", [(i, i ^ step) for i in range(count)])
        step *= 2
    return values


def dom_gather(values):
    count = lax.axis_size("dom")
    me = lax.axis_index("dom")
    values = values[None]
    step = 1
    while step < count:
        got = lax.ppermute(values, "dom", [(i, i ^ step) for i in range(count)])
        upper = (me // step) % 2 == 1
        values = jnp.where(
            upper, jnp.concatenate([got, values]), jnp.concatenate([values, got])
        )
        step *= 2
    return values


MESH_AXES = ("batch", "dom")
CORE0_BITS = (1, 3, 4, 2, 7, 5, 6)
CORE1_BITS = (4, 1, 3, 5, 2, 7, 6)


def mesh_psum(values):
    sizes = (lax.axis_size("batch"), lax.axis_size("dom"))
    if sizes != (16, 16):
        return lax.psum(values, MESH_AXES)
    count = 256
    me = lax.axis_index(MESH_AXES)
    core = me % 2
    steps = [(0, 0)] + list(zip(CORE0_BITS, CORE1_BITS))
    chosen = []
    for bit0, bit1 in steps:
        half = values.shape[0] // 2
        upper = jnp.where(core == 0, (me >> bit0) & 1, (me >> bit1) & 1) == 1
        low, high = values[:half], values[half:]
        send = jnp.where(upper, low, high)
        keep = jnp.where(upper, high, low)
        pairs = [(i, i ^ (1 << (bit0 if i % 2 == 0 else bit1))) for i in range(count)]
        values = keep + lax.ppermute(send, MESH_AXES, pairs)
        chosen.append((upper, pairs))
    wide = values.dtype
    values = values.astype(jnp.bfloat16)
    for upper, pairs in reversed(chosen):
        got = lax.ppermute(values, MESH_AXES, pairs)
        values = jnp.where(
            upper, jnp.concatenate([got, values]), jnp.concatenate([values, got])
        )
    return values.astype(wide)


def per_channel(values, group_width):
    return jnp.repeat(values, group_width, axis=-1)[:, None, None, :]


def body(
    inputs,
    saved_q,
    saved_k,
    saved_v,
    attended,
    out_cot,
    conv_weight,
    qkv_weight,
    out_weight,
    norm_gain,
    norm_shift,
):
    samples, row_count, col_count, chan_count = inputs.shape
    tok_count = row_count * col_count
    group_width = chan_count // GROUPS
    head_width = chan_count // HEADS
    score_scale = head_width ** (-0.5)
    count = row_count * col_count * group_width * lax.axis_size("dom")
    f32 = jnp.float32
    bf16 = jnp.bfloat16
    input_wide = inputs.astype(f32)
    grouped = input_wide.reshape(samples, row_count, col_count, GROUPS, group_width)
    group_sums = dom_psum(jnp.stack([grouped.sum((1, 2, 4)), (grouped * grouped).sum((1, 2, 4))]))
    group_mean = group_sums[0] / count
    group_var = group_sums[1] / count - group_mean * group_mean
    inv_std = lax.rsqrt(group_var + EPSILON)
    normed = (input_wide - per_channel(group_mean, group_width)) * per_channel(inv_std, group_width)
    pre_act = normed * norm_gain + norm_shift
    sigmoid_pre = jax.nn.sigmoid(pre_act)
    activated = (pre_act * sigmoid_pre).astype(bf16)
    padded = with_halo(activated, (("dom", 1),), 1)
    padded = jnp.pad(padded, ((0, 0), (0, 0), (1, 1), (0, 0)))

    def shifted(source, row_start, col_start):
        return source[
            :, row_start : row_start + row_count, col_start : col_start + col_count, :
        ].reshape(-1, chan_count)

    conv_sum = input_wide.reshape(-1, chan_count)
    for tap_index in range(9):
        row_off = tap_index // 3 - 1
        col_off = tap_index % 3 - 1
        conv_sum = conv_sum + jnp.dot(
            shifted(padded, 1 + row_off, 1 + col_off),
            conv_weight[tap_index],
            preferred_element_type=f32,
        )
    residual = conv_sum.astype(bf16)
    out_flat = out_cot.reshape(-1, chan_count)
    attended_flat = attended.reshape(-1, chan_count)
    out_grad = jnp.einsum("nc,nd->cd", attended_flat, out_flat, preferred_element_type=f32)
    d_attended = jnp.einsum("nd,cd->nc", out_flat, out_weight, preferred_element_type=f32).astype(
        bf16
    )

    def split_heads(values):
        return values.reshape(samples, -1, HEADS, head_width)

    def scores(left, right):
        return jnp.einsum("sqhd,skhd->shqk", left, right, preferred_element_type=f32) * score_scale

    q_rows = saved_q.reshape(samples, tok_count, chan_count)
    k_rows = saved_k.reshape(samples, tok_count, chan_count)
    v_rows = saved_v.reshape(samples, tok_count, chan_count)
    do_rows = d_attended.reshape(samples, tok_count, chan_count)
    q_heads = split_heads(q_rows)
    k_heads = split_heads(k_rows)
    v_heads = split_heads(v_rows)
    do_heads = split_heads(do_rows)
    row_dot = jnp.einsum(
        "sqhd,sqhd->sqh",
        split_heads(attended.reshape(samples, tok_count, chan_count)),
        do_heads,
        preferred_element_type=f32,
    )
    row_dot_t = row_dot.transpose(0, 2, 1)

    def grad_terms(query_heads, dout_heads, key_heads, value_heads, log_norm_t, dot_t):
        softmax_p = jnp.exp(scores(query_heads, key_heads) - log_norm_t[..., None])
        d_probs = jnp.einsum("sqhd,skhd->shqk", dout_heads, value_heads, preferred_element_type=f32)
        d_scores = (softmax_p * (d_probs - dot_t[..., None])).astype(bf16)
        return (softmax_p.astype(bf16), d_scores)

    row_max = jnp.full((samples, HEADS, tok_count), -jnp.inf, f32)
    row_total = jnp.zeros((samples, HEADS, tok_count), f32)
    kv_all = lax.all_gather(jnp.stack([k_rows, v_rows]), "dom", axis=2, tiled=True)
    residual, padded, kv_all = lax.optimization_barrier((residual, padded, kv_all))
    k_all = kv_all[0]
    logits = scores(q_heads, split_heads(k_all))
    new_max = logits.max(-1)
    row_total = row_total * jnp.exp(row_max - new_max) + jnp.exp(logits - new_max[..., None]).sum(
        -1
    )
    row_max, row_total = (new_max, row_total)
    log_norm = row_max + jnp.log(row_total)
    shard_piece = (
        k_all,
        kv_all[1],
    )
    key_heads = split_heads(shard_piece[0])
    value_heads = split_heads(shard_piece[1])
    p_half, d_scores = grad_terms(q_heads, do_heads, key_heads, value_heads, log_norm, row_dot_t)
    q_accum = jnp.einsum("shqk,skhd->sqhd", d_scores, key_heads, preferred_element_type=f32)
    stats_local = dom_gather(jnp.stack([log_norm.transpose(0, 2, 1), row_dot]))
    stats_all = stats_local.transpose(1, 2, 0, 3, 4).reshape(2, samples, -1, HEADS)
    qdo_all = lax.all_gather(jnp.stack([q_rows, do_rows]), "dom", axis=2, tiled=True)
    shard_piece = (qdo_all[0], qdo_all[1])
    query_heads = split_heads(shard_piece[0])
    dout_heads = split_heads(shard_piece[1])
    norm_piece = stats_all[0].transpose(0, 2, 1)
    dot_piece = stats_all[1].transpose(0, 2, 1)
    p_half, d_scores = grad_terms(query_heads, dout_heads, k_heads, v_heads, norm_piece, dot_piece)
    k_accum = jnp.einsum("shqk,sqhd->skhd", d_scores, query_heads, preferred_element_type=f32)
    v_accum = jnp.einsum("shqk,sqhd->skhd", p_half, dout_heads, preferred_element_type=f32)
    k_accum, v_accum = (k_accum, v_accum)
    k_grad = (k_accum * score_scale).astype(bf16).reshape(samples, tok_count, chan_count)
    v_grad = v_accum.astype(bf16).reshape(samples, tok_count, chan_count)
    q_grad = (q_accum * score_scale).astype(bf16).reshape(samples, tok_count, chan_count)
    proj_grad = jnp.concatenate([q_grad, k_grad, v_grad], axis=-1).reshape(-1, 3 * chan_count)
    qkv_local = jnp.einsum("nc,nd->cd", residual, proj_grad, preferred_element_type=f32)
    d_residual = (
        out_flat.astype(f32)
        + jnp.einsum("nd,cd->nc", proj_grad, qkv_weight, preferred_element_type=f32)
    ).astype(bf16)
    d_res_map = d_residual.reshape(samples, row_count, col_count, chan_count)
    d_padded = with_halo(d_res_map, (("dom", 1),), 1)
    d_padded = jnp.pad(d_padded, ((0, 0), (0, 0), (1, 1), (0, 0)))
    conv_parts = []
    d_act = jnp.zeros((samples * tok_count, chan_count), f32)
    for tap_index in range(9):
        row_off = tap_index // 3 - 1
        col_off = tap_index % 3 - 1
        conv_parts.append(
            jnp.einsum(
                "nc,nd->cd",
                shifted(padded, 1 + row_off, 1 + col_off),
                d_residual,
                preferred_element_type=f32,
            )
        )
        d_act = d_act + jnp.einsum(
            "nd,cd->nc",
            shifted(d_padded, 1 - row_off, 1 - col_off),
            conv_weight[tap_index],
            preferred_element_type=f32,
        )
    conv_local = jnp.stack(conv_parts)
    d_pre = (
        d_act.reshape(samples, row_count, col_count, chan_count)
        * sigmoid_pre
        * (1.0 + pre_act * (1.0 - sigmoid_pre))
    )
    gain_local = (d_pre * normed).sum((0, 1, 2))
    shift_local = d_pre.sum((0, 1, 2))
    scaled = d_pre * norm_gain
    scaled_groups = scaled.reshape(samples, row_count, col_count, GROUPS, group_width)
    product_groups = (scaled * normed).reshape(samples, row_count, col_count, GROUPS, group_width)
    back_sums = dom_psum(jnp.stack([scaled_groups.sum((1, 2, 4)), product_groups.sum((1, 2, 4))]))
    parts = (out_grad, qkv_local, conv_local, gain_local, shift_local)
    flat = jnp.concatenate([part.reshape(-1) for part in parts])
    flat, back_sums = lax.optimization_barrier((flat, back_sums))
    first = back_sums[0] / count
    second = back_sums[1] / count
    input_grad = (
        d_res_map.astype(f32)
        + per_channel(inv_std, group_width)
        * (scaled - per_channel(first, group_width) - normed * per_channel(second, group_width))
    ).astype(bf16)
    total = flat.shape[0]
    padded_len = -(-total // 32768) * 32768
    flat = mesh_psum(jnp.pad(flat, (0, padded_len - total)))
    pieces = []
    offset = 0
    for part in parts:
        pieces.append(flat[offset : offset + part.size].reshape(part.shape))
        offset += part.size
    out_grad, qkv_grad, conv_grad, gain_grad, shift_grad = pieces
    return (input_grad, conv_grad, qkv_grad, out_grad, gain_grad, shift_grad)


def solution(mesh):
    placed = (
        P("batch", "dom", None, None),
        P("batch", "dom", None, None),
        P("batch", "dom", None, None),
        P("batch", "dom", None, None),
        P("batch", "dom", None, None),
        P("batch", "dom", None, None),
        P(),
        P(),
        P(),
        P(),
        P(),
    )
    return jax.shard_map(
        body,
        mesh=mesh,
        in_specs=placed,
        out_specs=(P("batch", "dom", None, None), P(), P(), P(), P(), P()),
        check_vma=False,
    )
```

```python
import jax
import jax.numpy as jnp
from jax import lax
from jax.sharding import PartitionSpec as P

HEADS = 1
GROUPS = 32


EPSILON = 1e-05


def with_halo(cells, sides, width):
    for axis, dim in sides:
        count = lax.axis_size(axis)
        ends = count - 1
        head = lax.slice_in_dim(cells, 0, width, axis=dim)
        tail = lax.slice_in_dim(cells, cells.shape[dim] - width, cells.shape[dim], axis=dim)
        cells = jnp.concatenate(
            [
                lax.ppermute(tail, axis, [(i, (i + 1) % count) for i in range(ends)]),
                cells,
                lax.ppermute(head, axis, [((i + 1) % count, i) for i in range(ends)]),
            ],
            axis=dim,
        )
    return cells


def dom_psum(values):
    count = lax.axis_size("dom")
    step = 1
    while step < count:
        values = values + lax.ppermute(values, "dom", [(i, i ^ step) for i in range(count)])
        step *= 2
    return values


def dom_gather(values):
    count = lax.axis_size("dom")
    me = lax.axis_index("dom")
    values = values[None]
    step = 1
    while step < count:
        got = lax.ppermute(values, "dom", [(i, i ^ step) for i in range(count)])
        upper = (me // step) % 2 == 1
        values = jnp.where(
            upper, jnp.concatenate([got, values]), jnp.concatenate([values, got])
        )
        step *= 2
    return values


MESH_AXES = ("batch", "dom")
CORE0_BITS = (1, 3, 4, 2, 7, 5, 6)
CORE1_BITS = (4, 1, 3, 5, 2, 7, 6)


def mesh_psum(values):
    sizes = (lax.axis_size("batch"), lax.axis_size("dom"))
    if sizes != (16, 16):
        return lax.psum(values, MESH_AXES)
    count = 256
    me = lax.axis_index(MESH_AXES)
    core = me % 2
    steps = [(0, 0)] + list(zip(CORE0_BITS, CORE1_BITS))
    chosen = []
    for bit0, bit1 in steps:
        half = values.shape[0] // 2
        upper = jnp.where(core == 0, (me >> bit0) & 1, (me >> bit1) & 1) == 1
        low, high = values[:half], values[half:]
        send = jnp.where(upper, low, high)
        keep = jnp.where(upper, high, low)
        pairs = [(i, i ^ (1 << (bit0 if i % 2 == 0 else bit1))) for i in range(count)]
        values = keep + lax.ppermute(send, MESH_AXES, pairs)
        chosen.append((upper, pairs))
    wide = values.dtype
    values = values.astype(jnp.bfloat16)
    for upper, pairs in reversed(chosen):
        got = lax.ppermute(values, MESH_AXES, pairs)
        values = jnp.where(
            upper, jnp.concatenate([got, values]), jnp.concatenate([values, got])
        )
    return values.astype(wide)


def per_channel(values, group_width):
    return jnp.repeat(values, group_width, axis=-1)[:, None, None, :]


def body(
    inputs,
    saved_q,
    saved_k,
    saved_v,
    attended,
    out_cot,
    conv_weight,
    qkv_weight,
    out_weight,
    norm_gain,
    norm_shift,
):
    samples, row_count, col_count, chan_count = inputs.shape
    tok_count = row_count * col_count
    group_width = chan_count // GROUPS
    head_width = chan_count // HEADS
    score_scale = head_width ** (-0.5)
    count = row_count * col_count * group_width * lax.axis_size("dom")
    f32 = jnp.float32
    bf16 = jnp.bfloat16
    input_wide = inputs.astype(f32)
    grouped = input_wide.reshape(samples, row_count, col_count, GROUPS, group_width)
    group_sums = dom_psum(jnp.stack([grouped.sum((1, 2, 4)), (grouped * grouped).sum((1, 2, 4))]))
    group_mean = group_sums[0] / count
    group_var = group_sums[1] / count - group_mean * group_mean
    inv_std = lax.rsqrt(group_var + EPSILON)
    normed = (input_wide - per_channel(group_mean, group_width)) * per_channel(inv_std, group_width)
    pre_act = normed * norm_gain + norm_shift
    sigmoid_pre = jax.nn.sigmoid(pre_act)
    activated = (pre_act * sigmoid_pre).astype(bf16)
    padded = with_halo(activated, (("dom", 1),), 1)
    padded = jnp.pad(padded, ((0, 0), (0, 0), (1, 1), (0, 0)))

    def shifted(source, row_start, col_start):
        return source[
            :, row_start : row_start + row_count, col_start : col_start + col_count, :
        ].reshape(-1, chan_count)

    conv_sum = input_wide.reshape(-1, chan_count)
    for tap_index in range(9):
        row_off = tap_index // 3 - 1
        col_off = tap_index % 3 - 1
        conv_sum = conv_sum + jnp.dot(
            shifted(padded, 1 + row_off, 1 + col_off),
            conv_weight[tap_index],
            preferred_element_type=f32,
        )
    residual = conv_sum.astype(bf16)
    out_flat = out_cot.reshape(-1, chan_count)
    attended_flat = attended.reshape(-1, chan_count)
    out_grad = jnp.einsum("nc,nd->cd", attended_flat, out_flat, preferred_element_type=f32)
    d_attended = jnp.einsum("nd,cd->nc", out_flat, out_weight, preferred_element_type=f32).astype(
        bf16
    )

    def split_heads(values):
        return values.reshape(samples, -1, HEADS, head_width)

    def scores(left, right):
        return jnp.einsum("sqhd,skhd->shqk", left, right, preferred_element_type=f32) * score_scale

    q_rows = saved_q.reshape(samples, tok_count, chan_count)
    k_rows = saved_k.reshape(samples, tok_count, chan_count)
    v_rows = saved_v.reshape(samples, tok_count, chan_count)
    do_rows = d_attended.reshape(samples, tok_count, chan_count)
    q_heads = split_heads(q_rows)
    k_heads = split_heads(k_rows)
    v_heads = split_heads(v_rows)
    do_heads = split_heads(do_rows)
    row_dot = jnp.einsum(
        "sqhd,sqhd->sqh",
        split_heads(attended.reshape(samples, tok_count, chan_count)),
        do_heads,
        preferred_element_type=f32,
    )
    row_dot_t = row_dot.transpose(0, 2, 1)

    def grad_terms(query_heads, dout_heads, key_heads, value_heads, log_norm_t, dot_t):
        softmax_p = jnp.exp(scores(query_heads, key_heads) - log_norm_t[..., None])
        d_probs = jnp.einsum("sqhd,skhd->shqk", dout_heads, value_heads, preferred_element_type=f32)
        d_scores = (softmax_p * (d_probs - dot_t[..., None])).astype(bf16)
        return (softmax_p.astype(bf16), d_scores)

    row_max = jnp.full((samples, HEADS, tok_count), -jnp.inf, f32)
    row_total = jnp.zeros((samples, HEADS, tok_count), f32)
    kv_all = lax.all_gather(jnp.stack([k_rows, v_rows]), "dom", axis=2, tiled=True)
    residual, padded, kv_all = lax.optimization_barrier((residual, padded, kv_all))
    k_all = kv_all[0]
    logits = scores(q_heads, split_heads(k_all))
    new_max = logits.max(-1)
    row_total = row_total * jnp.exp(row_max - new_max) + jnp.exp(logits - new_max[..., None]).sum(
        -1
    )
    row_max, row_total = (new_max, row_total)
    log_norm = row_max + jnp.log(row_total)
    shard_piece = (
        k_all,
        kv_all[1],
    )
    key_heads = split_heads(shard_piece[0])
    value_heads = split_heads(shard_piece[1])
    p_half, d_scores = grad_terms(q_heads, do_heads, key_heads, value_heads, log_norm, row_dot_t)
    q_accum = jnp.einsum("shqk,skhd->sqhd", d_scores, key_heads, preferred_element_type=f32)
    stats_local = dom_gather(jnp.stack([log_norm.transpose(0, 2, 1), row_dot]))
    stats_all = stats_local.transpose(1, 2, 0, 3, 4).reshape(2, samples, -1, HEADS)
    qdo_all = lax.all_gather(jnp.stack([q_rows, do_rows]), "dom", axis=2, tiled=True)
    shard_piece = (qdo_all[0], qdo_all[1])
    query_heads = split_heads(shard_piece[0])
    dout_heads = split_heads(shard_piece[1])
    norm_piece = stats_all[0].transpose(0, 2, 1)
    dot_piece = stats_all[1].transpose(0, 2, 1)
    p_half, d_scores = grad_terms(query_heads, dout_heads, k_heads, v_heads, norm_piece, dot_piece)
    k_accum = jnp.einsum("shqk,sqhd->skhd", d_scores, query_heads, preferred_element_type=f32)
    v_accum = jnp.einsum("shqk,sqhd->skhd", p_half, dout_heads, preferred_element_type=f32)
    k_accum, v_accum = (k_accum, v_accum)
    k_grad = (k_accum * score_scale).astype(bf16).reshape(samples, tok_count, chan_count)
    v_grad = v_accum.astype(bf16).reshape(samples, tok_count, chan_count)
    q_grad = (q_accum * score_scale).astype(bf16).reshape(samples, tok_count, chan_count)
    proj_grad = jnp.concatenate([q_grad, k_grad, v_grad], axis=-1).reshape(-1, 3 * chan_count)
    qkv_local = jnp.einsum("nc,nd->cd", residual, proj_grad, preferred_element_type=f32)
    d_residual = (
        out_flat.astype(f32)
        + jnp.einsum("nd,cd->nc", proj_grad, qkv_weight, preferred_element_type=f32)
    ).astype(bf16)
    d_res_map = d_residual.reshape(samples, row_count, col_count, chan_count)
    d_padded = with_halo(d_res_map, (("dom", 1),), 1)
    d_padded = jnp.pad(d_padded, ((0, 0), (0, 0), (1, 1), (0, 0)))
    taps = [(tap_index // 3 - 1, tap_index % 3 - 1) for tap_index in range(9)]
    act_cols = jnp.concatenate(
        [shifted(padded, 1 + row_off, 1 + col_off) for row_off, col_off in taps], axis=1
    )
    res_cols = jnp.concatenate(
        [shifted(d_padded, 1 - row_off, 1 - col_off) for row_off, col_off in taps], axis=1
    )
    conv_local = jnp.einsum(
        "nk,nd->kd", act_cols, d_residual, preferred_element_type=f32
    ).reshape(9, chan_count, chan_count)
    weight_rows = conv_weight.transpose(0, 2, 1).reshape(9 * chan_count, chan_count)
    d_act = jnp.einsum("nk,kc->nc", res_cols, weight_rows, preferred_element_type=f32)
    d_pre = (
        d_act.reshape(samples, row_count, col_count, chan_count)
        * sigmoid_pre
        * (1.0 + pre_act * (1.0 - sigmoid_pre))
    )
    gain_local = (d_pre * normed).sum((0, 1, 2))
    shift_local = d_pre.sum((0, 1, 2))
    scaled = d_pre * norm_gain
    scaled_groups = scaled.reshape(samples, row_count, col_count, GROUPS, group_width)
    product_groups = (scaled * normed).reshape(samples, row_count, col_count, GROUPS, group_width)
    back_sums = dom_psum(jnp.stack([scaled_groups.sum((1, 2, 4)), product_groups.sum((1, 2, 4))]))
    parts = (out_grad, qkv_local, conv_local, gain_local, shift_local)
    flat = jnp.concatenate([part.reshape(-1) for part in parts])
    flat, back_sums = lax.optimization_barrier((flat, back_sums))
    first = back_sums[0] / count
    second = back_sums[1] / count
    input_grad = (
        d_res_map.astype(f32)
        + per_channel(inv_std, group_width)
        * (scaled - per_channel(first, group_width) - normed * per_channel(second, group_width))
    ).astype(bf16)
    total = flat.shape[0]
    padded_len = -(-total // 32768) * 32768
    flat = mesh_psum(jnp.pad(flat, (0, padded_len - total)))
    pieces = []
    offset = 0
    for part in parts:
        pieces.append(flat[offset : offset + part.size].reshape(part.shape))
        offset += part.size
    out_grad, qkv_grad, conv_grad, gain_grad, shift_grad = pieces
    return (input_grad, conv_grad, qkv_grad, out_grad, gain_grad, shift_grad)


def solution(mesh):
    placed = (
        P("batch", "dom", None, None),
        P("batch", "dom", None, None),
        P("batch", "dom", None, None),
        P("batch", "dom", None, None),
        P("batch", "dom", None, None),
        P("batch", "dom", None, None),
        P(),
        P(),
        P(),
        P(),
        P(),
    )
    return jax.shard_map(
        body,
        mesh=mesh,
        in_specs=placed,
        out_specs=(P("batch", "dom", None, None), P(), P(), P(), P(), P()),
        check_vma=False,
    )
```

```python
import jax
import jax.numpy as jnp
from jax import lax
from jax.sharding import PartitionSpec as P

HEADS = 1
GROUPS = 32


EPSILON = 1e-05


def with_halo(cells, sides, width):
    for axis, dim in sides:
        count = lax.axis_size(axis)
        ends = count - 1
        head = lax.slice_in_dim(cells, 0, width, axis=dim)
        tail = lax.slice_in_dim(cells, cells.shape[dim] - width, cells.shape[dim], axis=dim)
        cells = jnp.concatenate(
            [
                lax.ppermute(tail, axis, [(i, (i + 1) % count) for i in range(ends)]),
                cells,
                lax.ppermute(head, axis, [((i + 1) % count, i) for i in range(ends)]),
            ],
            axis=dim,
        )
    return cells


def dom_psum(values):
    count = lax.axis_size("dom")
    step = 1
    while step < count:
        values = values + lax.ppermute(values, "dom", [(i, i ^ step) for i in range(count)])
        step *= 2
    return values


def dom_gather(values):
    count = lax.axis_size("dom")
    me = lax.axis_index("dom")
    values = values[None]
    step = 1
    while step < count:
        got = lax.ppermute(values, "dom", [(i, i ^ step) for i in range(count)])
        upper = (me // step) % 2 == 1
        values = jnp.where(
            upper, jnp.concatenate([got, values]), jnp.concatenate([values, got])
        )
        step *= 2
    return values


MESH_AXES = ("batch", "dom")
CORE0_BITS = (1, 3, 4, 2, 7, 5, 6)
CORE1_BITS = (4, 1, 3, 5, 2, 7, 6)


def mesh_psum(values):
    sizes = (lax.axis_size("batch"), lax.axis_size("dom"))
    if sizes != (16, 16):
        return lax.psum(values, MESH_AXES)
    count = 256
    me = lax.axis_index(MESH_AXES)
    core = me % 2
    steps = [(0, 0)] + list(zip(CORE0_BITS, CORE1_BITS))
    chosen = []
    for step_index, (bit0, bit1) in enumerate(steps):
        half = values.shape[0] // 2
        upper = jnp.where(core == 0, (me >> bit0) & 1, (me >> bit1) & 1) == 1
        low, high = values[:half], values[half:]
        send = jnp.where(upper, low, high)
        keep = jnp.where(upper, high, low)
        pairs = [(i, i ^ (1 << (bit0 if i % 2 == 0 else bit1))) for i in range(count)]
        if step_index < 3:
            send = send.astype(jnp.bfloat16)
        values = keep + lax.ppermute(send, MESH_AXES, pairs).astype(keep.dtype)
        chosen.append((upper, pairs))
    wide = values.dtype
    values = values.astype(jnp.bfloat16)
    for upper, pairs in reversed(chosen):
        got = lax.ppermute(values, MESH_AXES, pairs)
        values = jnp.where(
            upper, jnp.concatenate([got, values]), jnp.concatenate([values, got])
        )
    return values.astype(wide)


def per_channel(values, group_width):
    return jnp.repeat(values, group_width, axis=-1)[:, None, None, :]


def body(
    inputs,
    saved_q,
    saved_k,
    saved_v,
    attended,
    out_cot,
    conv_weight,
    qkv_weight,
    out_weight,
    norm_gain,
    norm_shift,
):
    samples, row_count, col_count, chan_count = inputs.shape
    tok_count = row_count * col_count
    group_width = chan_count // GROUPS
    head_width = chan_count // HEADS
    score_scale = head_width ** (-0.5)
    count = row_count * col_count * group_width * lax.axis_size("dom")
    f32 = jnp.float32
    bf16 = jnp.bfloat16
    input_wide = inputs.astype(f32)
    grouped = input_wide.reshape(samples, row_count, col_count, GROUPS, group_width)
    group_sums = dom_psum(jnp.stack([grouped.sum((1, 2, 4)), (grouped * grouped).sum((1, 2, 4))]))
    group_mean = group_sums[0] / count
    group_var = group_sums[1] / count - group_mean * group_mean
    inv_std = lax.rsqrt(group_var + EPSILON)
    normed = (input_wide - per_channel(group_mean, group_width)) * per_channel(inv_std, group_width)
    pre_act = normed * norm_gain + norm_shift
    sigmoid_pre = jax.nn.sigmoid(pre_act)
    activated = (pre_act * sigmoid_pre).astype(bf16)
    padded = with_halo(activated, (("dom", 1),), 1)
    padded = jnp.pad(padded, ((0, 0), (0, 0), (1, 1), (0, 0)))

    def shifted(source, row_start, col_start):
        return source[
            :, row_start : row_start + row_count, col_start : col_start + col_count, :
        ].reshape(-1, chan_count)

    conv_sum = input_wide.reshape(-1, chan_count)
    for tap_index in range(9):
        row_off = tap_index // 3 - 1
        col_off = tap_index % 3 - 1
        conv_sum = conv_sum + jnp.dot(
            shifted(padded, 1 + row_off, 1 + col_off),
            conv_weight[tap_index],
            preferred_element_type=f32,
        )
    residual = conv_sum.astype(bf16)
    out_flat = out_cot.reshape(-1, chan_count)
    attended_flat = attended.reshape(-1, chan_count)
    out_grad = jnp.einsum("nc,nd->cd", attended_flat, out_flat, preferred_element_type=f32)
    d_attended = jnp.einsum("nd,cd->nc", out_flat, out_weight, preferred_element_type=f32).astype(
        bf16
    )

    def split_heads(values):
        return values.reshape(samples, -1, HEADS, head_width)

    def scores(left, right):
        return jnp.einsum("sqhd,skhd->shqk", left, right, preferred_element_type=f32) * score_scale

    q_rows = saved_q.reshape(samples, tok_count, chan_count)
    k_rows = saved_k.reshape(samples, tok_count, chan_count)
    v_rows = saved_v.reshape(samples, tok_count, chan_count)
    do_rows = d_attended.reshape(samples, tok_count, chan_count)
    q_heads = split_heads(q_rows)
    k_heads = split_heads(k_rows)
    v_heads = split_heads(v_rows)
    do_heads = split_heads(do_rows)
    row_dot = jnp.einsum(
        "sqhd,sqhd->sqh",
        split_heads(attended.reshape(samples, tok_count, chan_count)),
        do_heads,
        preferred_element_type=f32,
    )
    row_dot_t = row_dot.transpose(0, 2, 1)

    def grad_terms(query_heads, dout_heads, key_heads, value_heads, log_norm_t, dot_t):
        softmax_p = jnp.exp(scores(query_heads, key_heads) - log_norm_t[..., None])
        d_probs = jnp.einsum("sqhd,skhd->shqk", dout_heads, value_heads, preferred_element_type=f32)
        d_scores = (softmax_p * (d_probs - dot_t[..., None])).astype(bf16)
        return (softmax_p.astype(bf16), d_scores)

    row_max = jnp.full((samples, HEADS, tok_count), -jnp.inf, f32)
    row_total = jnp.zeros((samples, HEADS, tok_count), f32)
    kv_all = lax.all_gather(jnp.stack([k_rows, v_rows]), "dom", axis=2, tiled=True)
    residual, padded, kv_all = lax.optimization_barrier((residual, padded, kv_all))
    k_all = kv_all[0]
    logits = scores(q_heads, split_heads(k_all))
    new_max = logits.max(-1)
    row_total = row_total * jnp.exp(row_max - new_max) + jnp.exp(logits - new_max[..., None]).sum(
        -1
    )
    row_max, row_total = (new_max, row_total)
    log_norm = row_max + jnp.log(row_total)
    shard_piece = (
        k_all,
        kv_all[1],
    )
    key_heads = split_heads(shard_piece[0])
    value_heads = split_heads(shard_piece[1])
    p_half, d_scores = grad_terms(q_heads, do_heads, key_heads, value_heads, log_norm, row_dot_t)
    q_accum = jnp.einsum("shqk,skhd->sqhd", d_scores, key_heads, preferred_element_type=f32)
    stats_local = dom_gather(jnp.stack([log_norm.transpose(0, 2, 1), row_dot]))
    stats_all = stats_local.transpose(1, 2, 0, 3, 4).reshape(2, samples, -1, HEADS)
    qdo_all = lax.all_gather(jnp.stack([q_rows, do_rows]), "dom", axis=2, tiled=True)
    shard_piece = (qdo_all[0], qdo_all[1])
    query_heads = split_heads(shard_piece[0])
    dout_heads = split_heads(shard_piece[1])
    norm_piece = stats_all[0].transpose(0, 2, 1)
    dot_piece = stats_all[1].transpose(0, 2, 1)
    p_half, d_scores = grad_terms(query_heads, dout_heads, k_heads, v_heads, norm_piece, dot_piece)
    k_accum = jnp.einsum("shqk,sqhd->skhd", d_scores, query_heads, preferred_element_type=f32)
    v_accum = jnp.einsum("shqk,sqhd->skhd", p_half, dout_heads, preferred_element_type=f32)
    k_accum, v_accum = (k_accum, v_accum)
    k_grad = (k_accum * score_scale).astype(bf16).reshape(samples, tok_count, chan_count)
    v_grad = v_accum.astype(bf16).reshape(samples, tok_count, chan_count)
    q_grad = (q_accum * score_scale).astype(bf16).reshape(samples, tok_count, chan_count)
    proj_grad = jnp.concatenate([q_grad, k_grad, v_grad], axis=-1).reshape(-1, 3 * chan_count)
    qkv_local = jnp.einsum("nc,nd->cd", residual, proj_grad, preferred_element_type=f32)
    d_residual = (
        out_flat.astype(f32)
        + jnp.einsum("nd,cd->nc", proj_grad, qkv_weight, preferred_element_type=f32)
    ).astype(bf16)
    d_res_map = d_residual.reshape(samples, row_count, col_count, chan_count)
    d_padded = with_halo(d_res_map, (("dom", 1),), 1)
    d_padded = jnp.pad(d_padded, ((0, 0), (0, 0), (1, 1), (0, 0)))
    taps = [(tap_index // 3 - 1, tap_index % 3 - 1) for tap_index in range(9)]
    act_cols = jnp.concatenate(
        [shifted(padded, 1 + row_off, 1 + col_off) for row_off, col_off in taps], axis=1
    )
    res_cols = jnp.concatenate(
        [shifted(d_padded, 1 - row_off, 1 - col_off) for row_off, col_off in taps], axis=1
    )
    conv_local = jnp.einsum(
        "nk,nd->kd", act_cols, d_residual, preferred_element_type=f32
    ).reshape(9, chan_count, chan_count)
    weight_rows = conv_weight.transpose(0, 2, 1).reshape(9 * chan_count, chan_count)
    d_act = jnp.einsum("nk,kc->nc", res_cols, weight_rows, preferred_element_type=f32)
    d_pre = (
        d_act.reshape(samples, row_count, col_count, chan_count)
        * sigmoid_pre
        * (1.0 + pre_act * (1.0 - sigmoid_pre))
    )
    gain_local = (d_pre * normed).sum((0, 1, 2))
    shift_local = d_pre.sum((0, 1, 2))
    scaled = d_pre * norm_gain
    scaled_groups = scaled.reshape(samples, row_count, col_count, GROUPS, group_width)
    product_groups = (scaled * normed).reshape(samples, row_count, col_count, GROUPS, group_width)
    back_sums = dom_psum(jnp.stack([scaled_groups.sum((1, 2, 4)), product_groups.sum((1, 2, 4))]))
    parts = (out_grad, qkv_local, conv_local, gain_local, shift_local)
    flat = jnp.concatenate([part.reshape(-1) for part in parts])
    flat, back_sums = lax.optimization_barrier((flat, back_sums))
    first = back_sums[0] / count
    second = back_sums[1] / count
    input_grad = (
        d_res_map.astype(f32)
        + per_channel(inv_std, group_width)
        * (scaled - per_channel(first, group_width) - normed * per_channel(second, group_width))
    ).astype(bf16)
    total = flat.shape[0]
    padded_len = -(-total // 32768) * 32768
    flat = mesh_psum(jnp.pad(flat, (0, padded_len - total)))
    pieces = []
    offset = 0
    for part in parts:
        pieces.append(flat[offset : offset + part.size].reshape(part.shape))
        offset += part.size
    out_grad, qkv_grad, conv_grad, gain_grad, shift_grad = pieces
    return (input_grad, conv_grad, qkv_grad, out_grad, gain_grad, shift_grad)


def solution(mesh):
    placed = (
        P("batch", "dom", None, None),
        P("batch", "dom", None, None),
        P("batch", "dom", None, None),
        P("batch", "dom", None, None),
        P("batch", "dom", None, None),
        P("batch", "dom", None, None),
        P(),
        P(),
        P(),
        P(),
        P(),
    )
    return jax.shard_map(
        body,
        mesh=mesh,
        in_specs=placed,
        out_specs=(P("batch", "dom", None, None), P(), P(), P(), P(), P()),
        check_vma=False,
    )
```

```python
import jax
import jax.numpy as jnp
from jax import lax
from jax.sharding import PartitionSpec as P

HEADS = 1
GROUPS = 32


EPSILON = 1e-05


def with_halo(cells, sides, width):
    for axis, dim in sides:
        count = lax.axis_size(axis)
        ends = count - 1
        head = lax.slice_in_dim(cells, 0, width, axis=dim)
        tail = lax.slice_in_dim(cells, cells.shape[dim] - width, cells.shape[dim], axis=dim)
        cells = jnp.concatenate(
            [
                lax.ppermute(tail, axis, [(i, (i + 1) % count) for i in range(ends)]),
                cells,
                lax.ppermute(head, axis, [((i + 1) % count, i) for i in range(ends)]),
            ],
            axis=dim,
        )
    return cells


def dom_psum(values):
    count = lax.axis_size("dom")
    step = 1
    while step < count:
        values = values + lax.ppermute(values, "dom", [(i, i ^ step) for i in range(count)])
        step *= 2
    return values


def dom_gather(values):
    count = lax.axis_size("dom")
    me = lax.axis_index("dom")
    values = values[None]
    step = 1
    while step < count:
        got = lax.ppermute(values, "dom", [(i, i ^ step) for i in range(count)])
        upper = (me // step) % 2 == 1
        values = jnp.where(
            upper, jnp.concatenate([got, values]), jnp.concatenate([values, got])
        )
        step *= 2
    return values


MESH_AXES = ("batch", "dom")
CORE0_BITS = (1, 3, 4, 2, 7, 5, 6)
CORE1_BITS = (4, 1, 3, 5, 2, 7, 6)


def mesh_psum(values, rider):
    sizes = (lax.axis_size("batch"), lax.axis_size("dom"))
    if sizes != (16, 16):
        return lax.psum(values, MESH_AXES), rider
    count = 256
    me = lax.axis_index(MESH_AXES)
    core = me % 2
    steps = [(0, 0)] + list(zip(CORE0_BITS, CORE1_BITS))
    chosen = []
    for step_index, (bit0, bit1) in enumerate(steps):
        half = values.shape[0] // 2
        upper = jnp.where(core == 0, (me >> bit0) & 1, (me >> bit1) & 1) == 1
        low, high = values[:half], values[half:]
        send = jnp.where(upper, low, high)
        keep = jnp.where(upper, high, low)
        pairs = [(i, i ^ (1 << (bit0 if i % 2 == 0 else bit1))) for i in range(count)]
        if step_index < 3:
            send = send.astype(jnp.bfloat16)
        values = keep + lax.ppermute(send, MESH_AXES, pairs).astype(keep.dtype)
        if step_index == 1:
            values, rider = lax.optimization_barrier((values, rider))
        chosen.append((upper, pairs))
    wide = values.dtype
    values = values.astype(jnp.bfloat16)
    for upper, pairs in reversed(chosen):
        got = lax.ppermute(values, MESH_AXES, pairs)
        values = jnp.where(
            upper, jnp.concatenate([got, values]), jnp.concatenate([values, got])
        )
    return values.astype(wide), rider


def per_channel(values, group_width):
    return jnp.repeat(values, group_width, axis=-1)[:, None, None, :]


def body(
    inputs,
    saved_q,
    saved_k,
    saved_v,
    attended,
    out_cot,
    conv_weight,
    qkv_weight,
    out_weight,
    norm_gain,
    norm_shift,
):
    samples, row_count, col_count, chan_count = inputs.shape
    tok_count = row_count * col_count
    group_width = chan_count // GROUPS
    head_width = chan_count // HEADS
    score_scale = head_width ** (-0.5)
    count = row_count * col_count * group_width * lax.axis_size("dom")
    f32 = jnp.float32
    bf16 = jnp.bfloat16
    input_wide = inputs.astype(f32)
    grouped = input_wide.reshape(samples, row_count, col_count, GROUPS, group_width)
    group_sums = dom_psum(jnp.stack([grouped.sum((1, 2, 4)), (grouped * grouped).sum((1, 2, 4))]))
    group_mean = group_sums[0] / count
    group_var = group_sums[1] / count - group_mean * group_mean
    inv_std = lax.rsqrt(group_var + EPSILON)
    normed = (input_wide - per_channel(group_mean, group_width)) * per_channel(inv_std, group_width)
    pre_act = normed * norm_gain + norm_shift
    sigmoid_pre = jax.nn.sigmoid(pre_act)
    activated = (pre_act * sigmoid_pre).astype(bf16)
    padded = with_halo(activated, (("dom", 1),), 1)
    padded = jnp.pad(padded, ((0, 0), (0, 0), (1, 1), (0, 0)))

    def shifted(source, row_start, col_start):
        return source[
            :, row_start : row_start + row_count, col_start : col_start + col_count, :
        ].reshape(-1, chan_count)

    conv_sum = input_wide.reshape(-1, chan_count)
    for tap_index in range(9):
        row_off = tap_index // 3 - 1
        col_off = tap_index % 3 - 1
        conv_sum = conv_sum + jnp.dot(
            shifted(padded, 1 + row_off, 1 + col_off),
            conv_weight[tap_index],
            preferred_element_type=f32,
        )
    residual = conv_sum.astype(bf16)
    out_flat = out_cot.reshape(-1, chan_count)
    attended_flat = attended.reshape(-1, chan_count)
    out_grad = jnp.einsum("nc,nd->cd", attended_flat, out_flat, preferred_element_type=f32)
    d_attended = jnp.einsum("nd,cd->nc", out_flat, out_weight, preferred_element_type=f32).astype(
        bf16
    )

    def split_heads(values):
        return values.reshape(samples, -1, HEADS, head_width)

    def scores(left, right):
        return jnp.einsum("sqhd,skhd->shqk", left, right, preferred_element_type=f32) * score_scale

    q_rows = saved_q.reshape(samples, tok_count, chan_count)
    k_rows = saved_k.reshape(samples, tok_count, chan_count)
    v_rows = saved_v.reshape(samples, tok_count, chan_count)
    do_rows = d_attended.reshape(samples, tok_count, chan_count)
    q_heads = split_heads(q_rows)
    k_heads = split_heads(k_rows)
    v_heads = split_heads(v_rows)
    do_heads = split_heads(do_rows)
    row_dot = jnp.einsum(
        "sqhd,sqhd->sqh",
        split_heads(attended.reshape(samples, tok_count, chan_count)),
        do_heads,
        preferred_element_type=f32,
    )
    row_dot_t = row_dot.transpose(0, 2, 1)

    def grad_terms(query_heads, dout_heads, key_heads, value_heads, log_norm_t, dot_t):
        softmax_p = jnp.exp(scores(query_heads, key_heads) - log_norm_t[..., None])
        d_probs = jnp.einsum("sqhd,skhd->shqk", dout_heads, value_heads, preferred_element_type=f32)
        d_scores = (softmax_p * (d_probs - dot_t[..., None])).astype(bf16)
        return (softmax_p.astype(bf16), d_scores)

    row_max = jnp.full((samples, HEADS, tok_count), -jnp.inf, f32)
    row_total = jnp.zeros((samples, HEADS, tok_count), f32)
    kv_all = lax.all_gather(jnp.stack([k_rows, v_rows]), "dom", axis=2, tiled=True)
    residual, padded, kv_all = lax.optimization_barrier((residual, padded, kv_all))
    k_all = kv_all[0]
    logits = scores(q_heads, split_heads(k_all))
    new_max = logits.max(-1)
    row_total = row_total * jnp.exp(row_max - new_max) + jnp.exp(logits - new_max[..., None]).sum(
        -1
    )
    row_max, row_total = (new_max, row_total)
    log_norm = row_max + jnp.log(row_total)
    shard_piece = (
        k_all,
        kv_all[1],
    )
    key_heads = split_heads(shard_piece[0])
    value_heads = split_heads(shard_piece[1])
    p_half, d_scores = grad_terms(q_heads, do_heads, key_heads, value_heads, log_norm, row_dot_t)
    q_accum = jnp.einsum("shqk,skhd->sqhd", d_scores, key_heads, preferred_element_type=f32)
    stats_local = dom_gather(jnp.stack([log_norm.transpose(0, 2, 1), row_dot]))
    stats_all = stats_local.transpose(1, 2, 0, 3, 4).reshape(2, samples, -1, HEADS)
    qdo_all = lax.all_gather(jnp.stack([q_rows, do_rows]), "dom", axis=2, tiled=True)
    shard_piece = (qdo_all[0], qdo_all[1])
    query_heads = split_heads(shard_piece[0])
    dout_heads = split_heads(shard_piece[1])
    norm_piece = stats_all[0].transpose(0, 2, 1)
    dot_piece = stats_all[1].transpose(0, 2, 1)
    p_half, d_scores = grad_terms(query_heads, dout_heads, k_heads, v_heads, norm_piece, dot_piece)
    k_accum = jnp.einsum("shqk,sqhd->skhd", d_scores, query_heads, preferred_element_type=f32)
    v_accum = jnp.einsum("shqk,sqhd->skhd", p_half, dout_heads, preferred_element_type=f32)
    k_accum, v_accum = (k_accum, v_accum)
    k_grad = (k_accum * score_scale).astype(bf16).reshape(samples, tok_count, chan_count)
    v_grad = v_accum.astype(bf16).reshape(samples, tok_count, chan_count)
    q_grad = (q_accum * score_scale).astype(bf16).reshape(samples, tok_count, chan_count)
    proj_grad = jnp.concatenate([q_grad, k_grad, v_grad], axis=-1).reshape(-1, 3 * chan_count)
    qkv_local = jnp.einsum("nc,nd->cd", residual, proj_grad, preferred_element_type=f32)
    d_residual = (
        out_flat.astype(f32)
        + jnp.einsum("nd,cd->nc", proj_grad, qkv_weight, preferred_element_type=f32)
    ).astype(bf16)
    d_res_map = d_residual.reshape(samples, row_count, col_count, chan_count)
    d_padded = with_halo(d_res_map, (("dom", 1),), 1)
    d_padded = jnp.pad(d_padded, ((0, 0), (0, 0), (1, 1), (0, 0)))
    taps = [(tap_index // 3 - 1, tap_index % 3 - 1) for tap_index in range(9)]
    act_cols = jnp.concatenate(
        [shifted(padded, 1 + row_off, 1 + col_off) for row_off, col_off in taps], axis=1
    )
    res_cols = jnp.concatenate(
        [shifted(d_padded, 1 - row_off, 1 - col_off) for row_off, col_off in taps], axis=1
    )
    conv_local = jnp.einsum(
        "nk,nd->kd", act_cols, d_residual, preferred_element_type=f32
    ).reshape(9, chan_count, chan_count)
    weight_rows = conv_weight.transpose(0, 2, 1).reshape(9 * chan_count, chan_count)
    d_act = jnp.einsum("nk,kc->nc", res_cols, weight_rows, preferred_element_type=f32)
    d_pre = (
        d_act.reshape(samples, row_count, col_count, chan_count)
        * sigmoid_pre
        * (1.0 + pre_act * (1.0 - sigmoid_pre))
    )
    gain_local = (d_pre * normed).sum((0, 1, 2))
    shift_local = d_pre.sum((0, 1, 2))
    scaled = d_pre * norm_gain
    scaled_groups = scaled.reshape(samples, row_count, col_count, GROUPS, group_width)
    product_groups = (scaled * normed).reshape(samples, row_count, col_count, GROUPS, group_width)
    back_sums = dom_psum(jnp.stack([scaled_groups.sum((1, 2, 4)), product_groups.sum((1, 2, 4))]))
    parts = (out_grad, qkv_local, conv_local, gain_local, shift_local)
    flat = jnp.concatenate([part.reshape(-1) for part in parts])
    flat, back_sums = lax.optimization_barrier((flat, back_sums))
    first = back_sums[0] / count
    second = back_sums[1] / count
    input_grad = (
        d_res_map.astype(f32)
        + per_channel(inv_std, group_width)
        * (scaled - per_channel(first, group_width) - normed * per_channel(second, group_width))
    ).astype(bf16)
    total = flat.shape[0]
    padded_len = -(-total // 32768) * 32768
    flat, input_grad = mesh_psum(jnp.pad(flat, (0, padded_len - total)), input_grad)
    pieces = []
    offset = 0
    for part in parts:
        pieces.append(flat[offset : offset + part.size].reshape(part.shape))
        offset += part.size
    out_grad, qkv_grad, conv_grad, gain_grad, shift_grad = pieces
    return (input_grad, conv_grad, qkv_grad, out_grad, gain_grad, shift_grad)


def solution(mesh):
    placed = (
        P("batch", "dom", None, None),
        P("batch", "dom", None, None),
        P("batch", "dom", None, None),
        P("batch", "dom", None, None),
        P("batch", "dom", None, None),
        P("batch", "dom", None, None),
        P(),
        P(),
        P(),
        P(),
        P(),
    )
    return jax.shard_map(
        body,
        mesh=mesh,
        in_specs=placed,
        out_specs=(P("batch", "dom", None, None), P(), P(), P(), P(), P()),
        check_vma=False,
    )
```
